512 devices in a mesh: tensor: 8 (over y), expert: 64 (over x, z, core).
Axes of the slice: x: 4, y: 8, z: 8, core: 2. Of those that a mesh axis runs over, the one named last changes fastest.
Arguments:
- attn_partial: bfloat16 [8, 4096, 4096], P('tensor', 'expert'), may hold values from -6 to 6
- norm_gain: float32 [4096], replicated, may hold values from 0.1 to 1.9
- expert_ids: int32 [4096, 8], P('expert'), may hold values from 0 to 63, all different within a row; in each aligned block of 8 rows (0 to 7, 8 to 15, ...) at most 2 rows name the same one
- route_weights: float32 [4096, 8], P('expert'), may hold values from 0.1 to 1
- gate_proj: bfloat16 [64, 4096, 1024], P('expert', None, 'tensor'), may hold values from -0.09375 to 0.09375
- up_proj: bfloat16 [64, 4096, 1024], P('expert', None, 'tensor'), may hold values from -0.09375 to 0.09375
- down_proj: bfloat16 [64, 1024, 4096], P('expert', None, 'tensor'), may hold values from -0.1875 to 0.1875
Outputs:
- combined: bfloat16 [4096, 4096], P(('expert', 'tensor'))
The draws below stay inside these ranges and needn't reach their ends.
Inputs may be any that keep to these rules, and one draw needn't show every extreme that they name: `expert_ids`: each row names 8 different experts. In each aligned block of 8 rows (the rows of one device in the output's order) no expert is named by more than 2 rows, a bound that some block reaches.
All inputs are finite; a program needn't handle non-finite values.
Results may differ from the reference program's by a relative error of at most 0.025.
Values may be sent and summed in bfloat16 or wider, within the bound.
No kernel may reach another device: no remote copies, remote signals or barrier semaphores. Data moves between devices by JAX's collectives and lax.ppermute only.
A program may use at most 64 MiB of HBM per device.

```python
import math
import jax
import jax.numpy as jnp
import numpy as np
from jax import lax

D = 4096
H = 1024
TOP = 8
QB = 128
ROWS = 8
TOKENS = 4096
EXPERTS = 64
SHARDS = 8
CAP = 2
NB = 32


def block_levels(stream_key, dims, shards, smallest, largest):
    level, own = 1.0, jax.random.fold_in(stream_key, 6)
    for axis_at, shards_of in shards:
        heights = jnp.exp(jax.random.uniform(jax.random.fold_in(own, axis_at), (shards_of,), jnp.float32, smallest / len(shards), largest / len(shards)))
        level = level * jnp.repeat(heights, dims[axis_at] // shards_of).reshape([-1 if axis == axis_at else 1 for axis in range(len(dims))])
    return level


def shared_out(own_key, own, number, rows, amount, top, most, lean):
    ranking = jax.random.permutation(own_key, amount)
    packed, common = portions_of(amount, rows * top, most, lean, True), portions_of(amount, rows * top, most, lean, False)
    places = jnp.arange(amount)

    def named(sizes, turn):
        used = int((sizes > 0).sum())
        fixed = max(1, used // 4)
        shifted = fixed + (places - fixed + turn * (used - fixed)) % max(1, amount - fixed)
        return jnp.zeros((amount,), jnp.int32).at[ranking[jnp.where(places < fixed, places, shifted)]].set(jnp.asarray(sizes, jnp.int32))

    sizes = jnp.where(number % 4 == 0, named(packed, number // 4), named(common, number - number // 4 - 1))
    mixed = jax.random.permutation(jax.random.fold_in(own, 3), amount)
    giver, taker = mixed[0:amount // 2 * 2:2], mixed[1:amount // 2 * 2:2]
    margin = jnp.minimum(sizes[giver] - 1, most - sizes[taker]) // 2
    margin = jnp.where((giver == ranking[0]) | (taker == ranking[0]) | (sizes[taker] == 0), 0, jnp.maximum(margin, 0))
    shifted = jax.random.randint(jax.random.fold_in(own, 4), (amount // 2,), 0, 1 << 20) % (margin + 1)
    sizes = sizes.at[giver].add(-shifted).at[taker].add(shifted)
    items = jnp.searchsorted(jnp.cumsum(sizes), jnp.arange(rows * top), side="right").astype(jnp.int32)
    listing = items.reshape(top, rows).T
    listing = listing[jax.random.permutation(jax.random.fold_in(own, 1), rows)]
    turn = jax.random.randint(jax.random.fold_in(own, 2), (rows, 1), 0, top)
    return jnp.take_along_axis(listing, (jnp.arange(top)[None, :] + turn) % top, axis=1)


def portions_of(amount, total, most, slope, full):
    portions = [(1 << 20) // math.isqrt(standing ** slope) + 1 for standing in range(1, amount + 1)]
    largest = most if full else min(most, max(-(-total // amount), total * portions[0] // sum(portions)))
    least = 1 if total - largest >= amount - 1 else 0
    counts, rest = [largest] + [least] * (amount - 1), total - largest - least * (amount - 1)
    while rest > 0:
        candidates = [i for i in range(1, amount) if counts[i] < largest] or [i for i in range(1, amount) if counts[i] < most]
        pool, budget = sum([portions[i] for i in candidates]), rest
        for i in candidates:
            extra = min(most - counts[i], max(1, budget * portions[i] // pool), rest)
            counts[i] = counts[i] + extra
            rest = rest - extra
    return np.array(counts)


def centred(rng, dims, deviation, limit, split=(), kind=jnp.bfloat16):
    factor_of = block_levels(rng, dims, split, -0.22, 0.18) if split else 1.0
    values = jax.random.normal(rng, dims, jnp.float32) * deviation * factor_of
    return jnp.minimum(jnp.maximum(values, -limit), limit).astype(kind)


def setup_inputs(seed: int = 0) -> dict:
    streams_of = jax.random.split(jax.random.key(seed), 8)
    attn_partial = centred(streams_of[0], (SHARDS, TOKENS, D), 1.0, 6.0, ((0, 8), (1, 64)))
    norm_gain = jnp.clip(1.0 + 0.18 * jax.random.normal(streams_of[1], (D,), jnp.float32), 0.1, 1.9)
    expert_ids_keys = jax.random.split(jax.random.fold_in(streams_of[2], 1), TOKENS // ROWS)
    expert_ids_turns = jax.random.permutation(jax.random.fold_in(streams_of[2], 3), TOKENS // ROWS)
    expert_ids = jax.vmap(lambda own, number: shared_out(jax.random.fold_in(streams_of[2], 2), own, number, ROWS, EXPERTS, TOP, CAP, 2))(expert_ids_keys, expert_ids_turns).reshape((TOKENS, TOP))
    route_weights = jnp.clip(jnp.exp(math.log(1.0) - 2.3025851 * jax.random.uniform(streams_of[3], (TOKENS, TOP), jnp.float32) ** block_levels(streams_of[3], (TOKENS, TOP), ((0, 64),), -0.2, 0.2)), 0.1, 1.0)
    gate_proj = centred(streams_of[4], (EXPERTS, D, H), D ** -0.5, 0.09375, ((0, 64), (2, 8)))
    up_proj = centred(streams_of[5], (EXPERTS, D, H), D ** -0.5, 0.09375, ((0, 64), (2, 8)))
    down_proj = centred(streams_of[6], (EXPERTS, H, D), H ** -0.5, 0.1875, ((0, 64), (2, 8)))
    return dict(attn_partial=attn_partial, norm_gain=norm_gain, expert_ids=expert_ids, route_weights=route_weights, gate_proj=gate_proj, up_proj=up_proj, down_proj=down_proj)


def normalize_quantize(summed, norm_gain, block_width):
    row_count, feature_width = summed.shape
    mean_sq = lax.optimization_barrier(jnp.mean(summed * summed, axis=-1, keepdims=True))
    normed = summed * lax.rsqrt(mean_sq + 1e-06) * norm_gain
    blocks = normed.reshape(row_count, feature_width // block_width, block_width)
    scales = ((lax.optimization_barrier(jnp.max(jnp.abs(blocks), axis=-1)) + 1e-06) / 448.0).astype(jnp.bfloat16)
    values = (blocks / scales.astype(jnp.float32)[:, :, None]).astype(jnp.bfloat16)
    return (values.reshape(row_count, feature_width), scales)

def route_slots(grouped_ids, expert_total):
    labels = jnp.arange(expert_total, dtype=jnp.int32)
    member = lax.optimization_barrier(jnp.sum((grouped_ids[..., None] == labels).astype(jnp.int32), axis=-2))
    earlier = jnp.cumsum(member, axis=-2) - member
    return (member, earlier)

def reference(attn_partial, norm_gain, expert_ids, route_weights, gate_proj, up_proj, down_proj):
    summed = lax.optimization_barrier(jnp.sum(attn_partial.astype(jnp.float32), axis=0))
    token_total = summed.shape[0]
    values, scales = normalize_quantize(summed, norm_gain, QB)
    dequant = (values.astype(jnp.float32).reshape(token_total, NB, QB) * scales.astype(jnp.float32)[:, :, None]).astype(jnp.bfloat16)
    padded = jnp.concatenate([dequant.reshape(token_total, D), jnp.zeros((1, D), jnp.bfloat16)], axis=0)
    block_total = token_total // ROWS
    member, earlier = route_slots(expert_ids.reshape(block_total, ROWS, TOP), EXPERTS)
    labels = jnp.arange(EXPERTS, dtype=jnp.int32)
    pair_weight = lax.optimization_barrier(jnp.sum(jnp.where(expert_ids[..., None] == labels, route_weights[..., None], jnp.zeros((), route_weights.dtype)), axis=-2))
    pair_weight = pair_weight.reshape(block_total, ROWS, EXPERTS)
    block_index = jnp.arange(block_total, dtype=jnp.int32)[:, None, None]
    row_index = jnp.arange(ROWS, dtype=jnp.int32)[None, :, None]
    expert_index = jnp.arange(EXPERTS, dtype=jnp.int32)[None, None, :]
    shape_all = (block_total, ROWS, EXPERTS)
    target_expert = jnp.where(member > 0, jnp.broadcast_to(expert_index, shape_all), EXPERTS).astype(jnp.int32)
    target_slot = (block_index * CAP + earlier).astype(jnp.int32)
    token_index = jnp.broadcast_to(block_index * ROWS + row_index, shape_all).astype(jnp.int32)
    table = jnp.full((EXPERTS, block_total * CAP), token_total, jnp.int32)
    table = table.at[target_expert, target_slot].set(token_index, mode='drop')
    weight_table = jnp.zeros((EXPERTS, block_total * CAP), pair_weight.dtype)
    weight_table = weight_table.at[target_expert, target_slot].set(pair_weight, mode='drop')

    def one_expert(running, inputs_pair):
        slot_tokens, slot_weights, w_gate, w_up, w_down = inputs_pair
        gathered_rows = padded[slot_tokens]
        gate_act = jnp.dot(gathered_rows, w_gate, preferred_element_type=jnp.float32)
        up_act = jnp.dot(gathered_rows, w_up, preferred_element_type=jnp.float32)
        hidden = (jax.nn.silu(gate_act) * up_act).astype(jnp.bfloat16)
        expert_rows = jnp.dot(hidden, w_down, preferred_element_type=jnp.float32).astype(jnp.bfloat16)
        running = running.at[slot_tokens].add(slot_weights[:, None] * expert_rows.astype(jnp.float32))
        return (running, None)
    start_total = jnp.zeros((token_total + 1, D), jnp.float32)
    running, _ = lax.scan(one_expert, start_total, (table, weight_table, gate_proj, up_proj, down_proj))
    return running[:token_total].astype(jnp.bfloat16)
```

```python
import jax
import jax.numpy as jnp
from jax import lax
from jax.sharding import PartitionSpec as P

QB = 128


def normalize_dequant(summed, norm_gain, block_width):
    row_count, feature_width = summed.shape
    mean_sq = jnp.mean(summed * summed, axis=-1, keepdims=True)
    normed = summed * lax.rsqrt(mean_sq + 1e-06) * norm_gain
    blocks = normed.reshape(row_count, feature_width // block_width, block_width)
    scales = ((jnp.max(jnp.abs(blocks), axis=-1) + 1e-06) / 448.0).astype(jnp.bfloat16)
    scale_f = scales.astype(jnp.float32)[:, :, None]
    values = (blocks / scale_f).astype(jnp.bfloat16)
    restored = (values.astype(jnp.float32) * scale_f).astype(jnp.bfloat16)
    return restored.reshape(row_count, feature_width)


def on_device(attn_partial, norm_gain, expert_ids, route_weights, gate_proj, up_proj, down_proj):
    tensor_count = lax.axis_size("tensor")
    expert_count = lax.axis_size("expert")
    tensor_index = lax.axis_index("tensor")
    group_tokens = expert_ids.shape[0]
    top_count = expert_ids.shape[1]
    row_count = group_tokens // tensor_count
    feature_width = attn_partial.shape[2]
    capacity = max(2, (2 * row_count * top_count + expert_count - 1) // expert_count)
    gate_matrix = gate_proj[0]
    up_matrix = up_proj[0]
    down_matrix = down_proj[0]
    column_share = down_matrix.shape[1]
    own_start = tensor_index * row_count
    own_ids = lax.dynamic_slice_in_dim(expert_ids, own_start, row_count, 0)
    own_weights = lax.dynamic_slice_in_dim(route_weights, own_start, row_count, 0)

    parts = lax.all_to_all(
        attn_partial[0].reshape(tensor_count, row_count, feature_width),
        "tensor", split_axis=0, concat_axis=0, tiled=True,
    )
    summed = jnp.sum(parts.astype(jnp.float32), axis=0)
    restored = normalize_dequant(summed, norm_gain, QB)

    labels = jnp.arange(expert_count, dtype=jnp.int32)
    hit = own_ids[..., None] == labels
    member = jnp.sum(hit.astype(jnp.int32), axis=1)
    earlier = jnp.cumsum(member, axis=0) - member
    places = jnp.arange(capacity, dtype=jnp.int32)
    chosen = (earlier[..., None] == places) & (member[..., None] > 0)
    send = jnp.einsum(
        "rec,rd->ecd", chosen.astype(jnp.bfloat16), restored, preferred_element_type=jnp.float32
    ).astype(jnp.bfloat16)
    recv = lax.all_to_all(send, "expert", split_axis=0, concat_axis=0, tiled=True)
    rows = lax.all_gather(recv, "tensor", axis=0, tiled=False)
    slot_total = tensor_count * expert_count * capacity
    rows = rows.reshape(slot_total, feature_width)
    gate_act = jnp.dot(rows, gate_matrix, preferred_element_type=jnp.float32)
    up_act = jnp.dot(rows, up_matrix, preferred_element_type=jnp.float32)
    hidden = (jax.nn.silu(gate_act) * up_act).astype(jnp.bfloat16)
    expert_sum = jnp.dot(
        lax.all_gather(hidden, "tensor", axis=1, tiled=True),
        down_matrix,
        preferred_element_type=jnp.float32,
    )
    expert_rows = expert_sum.astype(jnp.bfloat16).reshape(
        tensor_count, expert_count, capacity, column_share
    )
    returned = lax.all_to_all(
        lax.all_to_all(expert_rows, "tensor", split_axis=0, concat_axis=3, tiled=True),
        "expert",
        split_axis=1,
        concat_axis=1,
        tiled=True,
    )
    returned = returned.reshape(expert_count, capacity, feature_width)
    pair_weight = jnp.sum(jnp.where(hit, own_weights[..., None], 0.0), axis=1)
    mixing = jnp.where(chosen, pair_weight[..., None], 0.0)
    combined = jnp.einsum(
        "rec,ecd->rd", mixing, returned.astype(jnp.float32), precision=lax.Precision.HIGHEST
    )
    return combined.astype(jnp.bfloat16)


def solution(mesh):
    return jax.shard_map(
        on_device,
        mesh=mesh,
        in_specs=(
            P("tensor", "expert", None),
            P(),
            P("expert", None),
            P("expert", None),
            P("expert", None, "tensor"),
            P("expert", None, "tensor"),
            P("expert", None, "tensor"),
        ),
        out_specs=P(("expert", "tensor"), None),
        check_vma=False,
    )
```

```python
import jax
import jax.numpy as jnp
from jax import lax
from jax.sharding import PartitionSpec as P

QB = 128


def normalize_dequant(summed, norm_gain, block_width):
    row_count, feature_width = summed.shape
    mean_sq = jnp.mean(summed * summed, axis=-1, keepdims=True)
    normed = summed * lax.rsqrt(mean_sq + 1e-06) * norm_gain
    blocks = normed.reshape(row_count, feature_width // block_width, block_width)
    scales = ((jnp.max(jnp.abs(blocks), axis=-1) + 1e-06) / 448.0).astype(jnp.bfloat16)
    scale_f = scales.astype(jnp.float32)[:, :, None]
    values = (blocks / scale_f).astype(jnp.bfloat16)
    restored = (values.astype(jnp.float32) * scale_f).astype(jnp.bfloat16)
    return restored.reshape(row_count, feature_width)


def on_device(attn_partial, norm_gain, expert_ids, route_weights, gate_proj, up_proj, down_proj):
    tensor_count = lax.axis_size("tensor")
    expert_count = lax.axis_size("expert")
    tensor_index = lax.axis_index("tensor")
    group_tokens = expert_ids.shape[0]
    top_count = expert_ids.shape[1]
    row_count = group_tokens // tensor_count
    feature_width = attn_partial.shape[2]
    capacity = max(2, (2 * row_count * top_count + expert_count - 1) // expert_count)
    gate_matrix = gate_proj[0]
    up_matrix = up_proj[0]
    down_matrix = down_proj[0]
    column_share = down_matrix.shape[1]
    own_start = tensor_index * row_count
    own_ids = lax.dynamic_slice_in_dim(expert_ids, own_start, row_count, 0)
    own_weights = lax.dynamic_slice_in_dim(route_weights, own_start, row_count, 0)

    parts = lax.all_to_all(
        attn_partial[0].reshape(tensor_count, row_count, feature_width),
        "tensor", split_axis=0, concat_axis=0, tiled=True,
    )
    summed = jnp.sum(parts.astype(jnp.float32), axis=0)
    restored = normalize_dequant(summed, norm_gain, QB)

    labels = jnp.arange(expert_count, dtype=jnp.int32)
    hit = own_ids[..., None] == labels
    member = jnp.sum(hit.astype(jnp.int32), axis=1)
    earlier = jnp.cumsum(member, axis=0) - member
    places = jnp.arange(capacity, dtype=jnp.int32)
    chosen = (earlier[..., None] == places) & (member[..., None] > 0)
    send = jnp.einsum(
        "rec,rd->ecd", chosen.astype(jnp.bfloat16), restored, preferred_element_type=jnp.float32
    ).astype(jnp.bfloat16)
    recv = lax.all_to_all(send, "expert", split_axis=0, concat_axis=0, tiled=True)
    rows = lax.all_gather(
        recv.reshape(expert_count * capacity, feature_width), "tensor", axis=0, tiled=True
    )
    gate_act = jnp.dot(rows, gate_matrix, preferred_element_type=jnp.float32)
    up_act = jnp.dot(rows, up_matrix, preferred_element_type=jnp.float32)
    hidden = (jax.nn.silu(gate_act) * up_act).astype(jnp.bfloat16)
    hidden_all = lax.all_gather(hidden, "tensor", axis=0, tiled=False)
    expert_sum = jnp.einsum(
        "tsh,thc->sc",
        hidden_all,
        down_matrix.reshape(tensor_count, -1, column_share),
        preferred_element_type=jnp.float32,
    )
    expert_rows = expert_sum.astype(jnp.bfloat16).reshape(
        tensor_count, expert_count, capacity, column_share
    )
    returned = lax.all_to_all(
        lax.all_to_all(expert_rows, "tensor", split_axis=0, concat_axis=3, tiled=True),
        "expert",
        split_axis=1,
        concat_axis=1,
        tiled=True,
    )
    returned = returned.reshape(expert_count, capacity, feature_width)
    pair_weight = jnp.sum(jnp.where(hit, own_weights[..., None], 0.0), axis=1)
    mixing = jnp.where(chosen, pair_weight[..., None], 0.0)
    combined = jnp.einsum(
        "rec,ecd->rd", mixing, returned.astype(jnp.float32), precision=lax.Precision.HIGHEST
    )
    return combined.astype(jnp.bfloat16)


def solution(mesh):
    return jax.shard_map(
        on_device,
        mesh=mesh,
        in_specs=(
            P("tensor", "expert", None),
            P(),
            P("expert", None),
            P("expert", None),
            P("expert", None, "tensor"),
            P("expert", None, "tensor"),
            P("expert", None, "tensor"),
        ),
        out_specs=P(("expert", "tensor"), None),
        check_vma=False,
    )
```

```python
import jax
import jax.numpy as jnp
from jax import lax
from jax.sharding import PartitionSpec as P

QB = 128


def normalize_dequant(summed, norm_gain, block_width):
    row_count, feature_width = summed.shape
    mean_sq = jnp.mean(summed * summed, axis=-1, keepdims=True)
    normed = summed * lax.rsqrt(mean_sq + 1e-06) * norm_gain
    blocks = normed.reshape(row_count, feature_width // block_width, block_width)
    scales = ((jnp.max(jnp.abs(blocks), axis=-1) + 1e-06) / 448.0).astype(jnp.bfloat16)
    scale_f = scales.astype(jnp.float32)[:, :, None]
    values = (blocks / scale_f).astype(jnp.bfloat16)
    restored = (values.astype(jnp.float32) * scale_f).astype(jnp.bfloat16)
    return restored.reshape(row_count, feature_width)


def on_device(attn_partial, norm_gain, expert_ids, route_weights, gate_proj, up_proj, down_proj):
    tensor_count = lax.axis_size("tensor")
    expert_count = lax.axis_size("expert")
    tensor_index = lax.axis_index("tensor")
    group_tokens = expert_ids.shape[0]
    top_count = expert_ids.shape[1]
    row_count = group_tokens // tensor_count
    feature_width = attn_partial.shape[2]
    capacity = max(2, (2 * row_count * top_count + expert_count - 1) // expert_count)
    gate_matrix = gate_proj[0]
    up_matrix = up_proj[0]
    down_matrix = down_proj[0]
    own_start = tensor_index * row_count
    own_ids = lax.dynamic_slice_in_dim(expert_ids, own_start, row_count, 0)
    own_weights = lax.dynamic_slice_in_dim(route_weights, own_start, row_count, 0)

    parts = lax.all_to_all(
        attn_partial[0].reshape(tensor_count, row_count, feature_width),
        "tensor", split_axis=0, concat_axis=0, tiled=True,
    )
    summed = jnp.sum(parts.astype(jnp.float32), axis=0)
    restored = normalize_dequant(summed, norm_gain, QB)

    labels = jnp.arange(expert_count, dtype=jnp.int32)
    hit = own_ids[..., None] == labels
    member = jnp.sum(hit.astype(jnp.int32), axis=1)
    earlier = jnp.cumsum(member, axis=0) - member
    places = jnp.arange(capacity, dtype=jnp.int32)
    chosen = (earlier[..., None] == places) & (member[..., None] > 0)
    send = jnp.einsum(
        "rec,rd->ecd", chosen.astype(jnp.bfloat16), restored, preferred_element_type=jnp.float32
    ).astype(jnp.bfloat16)
    recv = lax.all_to_all(send, "expert", split_axis=0, concat_axis=0, tiled=True)
    down_all = lax.all_gather(down_matrix, "tensor", axis=0, tiled=False)
    down_all, recv = lax.optimization_barrier((down_all, recv))
    rows = lax.all_gather(
        recv.reshape(expert_count * capacity, feature_width), "tensor", axis=0, tiled=True
    )
    gate_act = jnp.dot(rows, gate_matrix, preferred_element_type=jnp.float32)
    up_act = jnp.dot(rows, up_matrix, preferred_element_type=jnp.float32)
    hidden = (jax.nn.silu(gate_act) * up_act).astype(jnp.bfloat16)
    hidden_own = lax.all_to_all(
        hidden.reshape(tensor_count, expert_count * capacity, -1),
        "tensor", split_axis=0, concat_axis=2, tiled=True,
    )[0]
    expert_sum = jnp.einsum(
        "sh,thc->stc", hidden_own, down_all, preferred_element_type=jnp.float32
    )
    expert_rows = expert_sum.astype(jnp.bfloat16).reshape(expert_count, capacity, feature_width)
    returned = lax.all_to_all(expert_rows, "expert", split_axis=0, concat_axis=0, tiled=True)
    returned = returned.reshape(expert_count, capacity, feature_width)
    pair_weight = jnp.sum(jnp.where(hit, own_weights[..., None], 0.0), axis=1)
    mixing = jnp.where(chosen, pair_weight[..., None], 0.0)
    combined = jnp.einsum(
        "rec,ecd->rd", mixing, returned.astype(jnp.float32), precision=lax.Precision.HIGHEST
    )
    return combined.astype(jnp.bfloat16)


def solution(mesh):
    return jax.shard_map(
        on_device,
        mesh=mesh,
        in_specs=(
            P("tensor", "expert", None),
            P(),
            P("expert", None),
            P("expert", None),
            P("expert", None, "tensor"),
            P("expert", None, "tensor"),
            P("expert", None, "tensor"),
        ),
        out_specs=P(("expert", "tensor"), None),
        check_vma=False,
    )
```

```python
import jax
import jax.numpy as jnp
from jax import lax
from jax.sharding import PartitionSpec as P

QB = 128


def normalize_dequant(summed, norm_gain, block_width):
    row_count, feature_width = summed.shape
    mean_sq = jnp.mean(summed * summed, axis=-1, keepdims=True)
    normed = summed * lax.rsqrt(mean_sq + 1e-06) * norm_gain
    blocks = normed.reshape(row_count, feature_width // block_width, block_width)
    scales = ((jnp.max(jnp.abs(blocks), axis=-1) + 1e-06) / 448.0).astype(jnp.bfloat16)
    scale_f = scales.astype(jnp.float32)[:, :, None]
    values = (blocks / scale_f).astype(jnp.bfloat16)
    restored = (values.astype(jnp.float32) * scale_f).astype(jnp.bfloat16)
    return restored.reshape(row_count, feature_width)


def on_device(attn_partial, norm_gain, expert_ids, route_weights, gate_proj, up_proj, down_proj):
    tensor_count = lax.axis_size("tensor")
    expert_count = lax.axis_size("expert")
    tensor_index = lax.axis_index("tensor")
    group_tokens = expert_ids.shape[0]
    top_count = expert_ids.shape[1]
    row_count = group_tokens // tensor_count
    feature_width = attn_partial.shape[2]
    capacity = max(2, (2 * row_count * top_count + expert_count - 1) // expert_count)
    gate_matrix = gate_proj[0]
    up_matrix = up_proj[0]
    down_matrix = down_proj[0]
    own_start = tensor_index * row_count
    own_ids = lax.dynamic_slice_in_dim(expert_ids, own_start, row_count, 0)
    own_weights = lax.dynamic_slice_in_dim(route_weights, own_start, row_count, 0)

    parts = lax.all_to_all(
        attn_partial[0].reshape(tensor_count, row_count, feature_width),
        "tensor", split_axis=0, concat_axis=0, tiled=True,
    )
    summed = jnp.sum(parts.astype(jnp.float32), axis=0)
    restored = normalize_dequant(summed, norm_gain, QB)

    labels = jnp.arange(expert_count, dtype=jnp.int32)
    hit = own_ids[..., None] == labels
    member = jnp.sum(hit.astype(jnp.int32), axis=1)
    earlier = jnp.cumsum(member, axis=0) - member
    places = jnp.arange(capacity, dtype=jnp.int32)
    chosen = (earlier[..., None] == places) & (member[..., None] > 0)
    send = jnp.einsum(
        "rec,rd->ecd", chosen.astype(jnp.bfloat16), restored, preferred_element_type=jnp.float32
    ).astype(jnp.bfloat16)
    recv = lax.all_to_all(send, "expert", split_axis=0, concat_axis=0, tiled=True)
    pieces = [down_matrix] + [None] * (tensor_count - 1)
    ahead = down_matrix
    behind = down_matrix
    for step in range(1, tensor_count // 2 + 1):
        ahead = lax.ppermute(ahead, "tensor", [(i, (i + 1) % tensor_count) for i in range(tensor_count)])
        pieces[tensor_count - step] = ahead
        if step < tensor_count - step:
            behind = lax.ppermute(behind, "tensor", [(i, (i - 1) % tensor_count) for i in range(tensor_count)])
            pieces[step] = behind
    pieces, recv = lax.optimization_barrier((pieces, recv))
    down_ring = jnp.stack(pieces)
    rows = lax.all_gather(
        recv.reshape(expert_count * capacity, feature_width), "tensor", axis=0, tiled=True
    )
    gate_act = jnp.dot(rows, gate_matrix, preferred_element_type=jnp.float32)
    up_act = jnp.dot(rows, up_matrix, preferred_element_type=jnp.float32)
    hidden = (jax.nn.silu(gate_act) * up_act).astype(jnp.bfloat16)
    hidden_own = lax.all_to_all(
        hidden.reshape(tensor_count, expert_count * capacity, -1),
        "tensor", split_axis=0, concat_axis=2, tiled=True,
    )[0]
    expert_sum = jnp.einsum(
        "sh,mhc->smc", hidden_own, down_ring, preferred_element_type=jnp.float32
    ).astype(jnp.bfloat16)
    expert_sum = jnp.roll(expert_sum, tensor_index, axis=1)
    expert_rows = expert_sum.reshape(expert_count, capacity, feature_width)
    returned = lax.all_to_all(expert_rows, "expert", split_axis=0, concat_axis=0, tiled=True)
    returned = returned.reshape(expert_count, capacity, feature_width)
    pair_weight = jnp.sum(jnp.where(hit, own_weights[..., None], 0.0), axis=1)
    mixing = jnp.where(chosen, pair_weight[..., None], 0.0)
    combined = jnp.einsum(
        "rec,ecd->rd", mixing, returned.astype(jnp.float32), precision=lax.Precision.HIGHEST
    )
    return combined.astype(jnp.bfloat16)


def solution(mesh):
    return jax.shard_map(
        on_device,
        mesh=mesh,
        in_specs=(
            P("tensor", "expert", None),
            P(),
            P("expert", None),
            P("expert", None),
            P("expert", None, "tensor"),
            P("expert", None, "tensor"),
            P("expert", None, "tensor"),
        ),
        out_specs=P(("expert", "tensor"), None),
        check_vma=False,
    )
```

```python
import jax
import jax.numpy as jnp
from jax import lax
from jax.sharding import PartitionSpec as P

QB = 128


def normalize_dequant(summed, norm_gain, block_width):
    row_count, feature_width = summed.shape
    mean_sq = jnp.mean(summed * summed, axis=-1, keepdims=True)
    normed = summed * lax.rsqrt(mean_sq + 1e-06) * norm_gain
    blocks = normed.reshape(row_count, feature_width // block_width, block_width)
    scales = ((jnp.max(jnp.abs(blocks), axis=-1) + 1e-06) / 448.0).astype(jnp.bfloat16)
    scale_f = scales.astype(jnp.float32)[:, :, None]
    values = (blocks / scale_f).astype(jnp.bfloat16)
    restored = (values.astype(jnp.float32) * scale_f).astype(jnp.bfloat16)
    return restored.reshape(row_count, feature_width)


def on_device(attn_partial, norm_gain, expert_ids, route_weights, gate_proj, up_proj, down_proj):
    tensor_count = lax.axis_size("tensor")
    expert_count = lax.axis_size("expert")
    tensor_index = lax.axis_index("tensor")
    group_tokens = expert_ids.shape[0]
    top_count = expert_ids.shape[1]
    row_count = group_tokens // tensor_count
    feature_width = attn_partial.shape[2]
    capacity = max(2, (2 * row_count * top_count + expert_count - 1) // expert_count)
    gate_matrix = gate_proj[0]
    up_matrix = up_proj[0]
    down_matrix = down_proj[0]
    own_start = tensor_index * row_count
    own_ids = lax.dynamic_slice_in_dim(expert_ids, own_start, row_count, 0)
    own_weights = lax.dynamic_slice_in_dim(route_weights, own_start, row_count, 0)

    parts = lax.all_to_all(
        attn_partial[0].reshape(tensor_count, row_count, feature_width),
        "tensor", split_axis=0, concat_axis=0, tiled=True,
    )
    summed = jnp.sum(parts.astype(jnp.float32), axis=0)
    restored = normalize_dequant(summed, norm_gain, QB)

    labels = jnp.arange(expert_count, dtype=jnp.int32)
    hit = own_ids[..., None] == labels
    member = jnp.sum(hit.astype(jnp.int32), axis=1)
    earlier = jnp.cumsum(member, axis=0) - member
    places = jnp.arange(capacity, dtype=jnp.int32)
    chosen = (earlier[..., None] == places) & (member[..., None] > 0)
    send = jnp.einsum(
        "rec,rd->ecd", chosen.astype(jnp.bfloat16), restored, preferred_element_type=jnp.float32
    ).astype(jnp.bfloat16)
    recv = lax.all_to_all(send, "expert", split_axis=0, concat_axis=0, tiled=True)
    down_all = lax.all_gather(down_matrix, "tensor", axis=0, tiled=False)
    def front(piece):
        gate_act = jnp.dot(piece, gate_matrix, preferred_element_type=jnp.float32)
        up_act = jnp.dot(piece, up_matrix, preferred_element_type=jnp.float32)
        return (jax.nn.silu(gate_act) * up_act).astype(jnp.bfloat16)

    own_rows = recv.reshape(expert_count * capacity, feature_width)
    hidden_parts = [front(own_rows)] + [None] * (tensor_count - 1)
    ahead = own_rows
    behind = own_rows
    for step in range(1, tensor_count // 2 + 1):
        ahead = lax.ppermute(ahead, "tensor", [(i, (i + 1) % tensor_count) for i in range(tensor_count)])
        hidden_parts[tensor_count - step] = front(ahead)
        if step < tensor_count - step:
            behind = lax.ppermute(behind, "tensor", [(i, (i - 1) % tensor_count) for i in range(tensor_count)])
            hidden_parts[step] = front(behind)
    hidden = jnp.roll(jnp.stack(hidden_parts), tensor_index, axis=0)
    hidden_own = lax.all_to_all(
        hidden.reshape(tensor_count, expert_count * capacity, -1),
        "tensor", split_axis=0, concat_axis=2, tiled=True,
    )[0]
    expert_sum = jnp.einsum(
        "sh,thc->stc", hidden_own, down_all, preferred_element_type=jnp.float32
    )
    expert_rows = expert_sum.astype(jnp.bfloat16).reshape(expert_count, capacity, feature_width)
    returned = lax.all_to_all(expert_rows, "expert", split_axis=0, concat_axis=0, tiled=True)
    returned = returned.reshape(expert_count, capacity, feature_width)
    pair_weight = jnp.sum(jnp.where(hit, own_weights[..., None], 0.0), axis=1)
    mixing = jnp.where(chosen, pair_weight[..., None], 0.0)
    combined = jnp.einsum(
        "rec,ecd->rd", mixing, returned.astype(jnp.float32), precision=lax.Precision.HIGHEST
    )
    return combined.astype(jnp.bfloat16)


def solution(mesh):
    return jax.shard_map(
        on_device,
        mesh=mesh,
        in_specs=(
            P("tensor", "expert", None),
            P(),
            P("expert", None),
            P("expert", None),
            P("expert", None, "tensor"),
            P("expert", None, "tensor"),
            P("expert", None, "tensor"),
        ),
        out_specs=P(("expert", "tensor"), None),
        check_vma=False,
    )
```

```python
import jax
import jax.numpy as jnp
from jax import lax
from jax.sharding import PartitionSpec as P

QB = 128


def normalize_dequant(summed, norm_gain, block_width):
    row_count, feature_width = summed.shape
    mean_sq = jnp.mean(summed * summed, axis=-1, keepdims=True)
    normed = summed * lax.rsqrt(mean_sq + 1e-06) * norm_gain
    blocks = normed.reshape(row_count, feature_width // block_width, block_width)
    scales = ((jnp.max(jnp.abs(blocks), axis=-1) + 1e-06) / 448.0).astype(jnp.bfloat16)
    scale_f = scales.astype(jnp.float32)[:, :, None]
    values = (blocks / scale_f).astype(jnp.bfloat16)
    restored = (values.astype(jnp.float32) * scale_f).astype(jnp.bfloat16)
    return restored.reshape(row_count, feature_width)


def on_device(attn_partial, norm_gain, expert_ids, route_weights, gate_proj, up_proj, down_proj):
    tensor_count = lax.axis_size("tensor")
    expert_count = lax.axis_size("expert")
    tensor_index = lax.axis_index("tensor")
    group_tokens = expert_ids.shape[0]
    top_count = expert_ids.shape[1]
    row_count = group_tokens // tensor_count
    feature_width = attn_partial.shape[2]
    capacity = max(2, (2 * row_count * top_count + expert_count - 1) // expert_count)
    gate_matrix = gate_proj[0]
    up_matrix = up_proj[0]
    down_matrix = down_proj[0]
    own_start = tensor_index * row_count
    own_ids = lax.dynamic_slice_in_dim(expert_ids, own_start, row_count, 0)
    own_weights = lax.dynamic_slice_in_dim(route_weights, own_start, row_count, 0)

    parts = lax.all_to_all(
        attn_partial[0].reshape(tensor_count, row_count, feature_width),
        "tensor", split_axis=0, concat_axis=0, tiled=True,
    )
    summed = jnp.sum(parts.astype(jnp.float32), axis=0)
    restored = normalize_dequant(summed, norm_gain, QB)

    labels = jnp.arange(expert_count, dtype=jnp.int32)
    hit = own_ids[..., None] == labels
    member = jnp.sum(hit.astype(jnp.int32), axis=1)
    earlier = jnp.cumsum(member, axis=0) - member
    places = jnp.arange(capacity, dtype=jnp.int32)
    chosen = (earlier[..., None] == places) & (member[..., None] > 0)
    send = jnp.einsum(
        "rec,rd->ecd", chosen.astype(jnp.bfloat16), restored, preferred_element_type=jnp.float32
    ).astype(jnp.bfloat16)
    recv = lax.all_to_all(send, "expert", split_axis=0, concat_axis=0, tiled=True)
    down_all = lax.all_gather(down_matrix, "tensor", axis=0, tiled=False)
    def front(piece):
        gate_act = jnp.dot(piece, gate_matrix, preferred_element_type=jnp.float32)
        up_act = jnp.dot(piece, up_matrix, preferred_element_type=jnp.float32)
        return (jax.nn.silu(gate_act) * up_act).astype(jnp.bfloat16)

    down_all, recv = lax.optimization_barrier((down_all, recv))
    own_rows = recv.reshape(expert_count * capacity, feature_width)
    hidden_parts = [front(own_rows)] + [None] * (tensor_count - 1)
    ahead = own_rows
    behind = own_rows
    forward = [(i, (i + 1) % tensor_count) for i in range(tensor_count)]
    backward = [(i, (i - 1) % tensor_count) for i in range(tensor_count)]
    half = own_rows.shape[0] // 2
    for step in range(1, tensor_count // 2 + 1):
        if step < tensor_count - step:
            ahead = lax.ppermute(ahead, "tensor", forward)
            hidden_parts[tensor_count - step] = front(ahead)
            behind = lax.ppermute(behind, "tensor", backward)
            hidden_parts[step] = front(behind)
        else:
            first = lax.ppermute(ahead[:half], "tensor", forward)
            second = lax.ppermute(behind[half:], "tensor", backward)
            hidden_parts[step] = jnp.concatenate([front(first), front(second)], axis=0)
    hidden = jnp.roll(jnp.stack(hidden_parts), tensor_index, axis=0)
    hidden_own = lax.all_to_all(
        hidden.reshape(tensor_count, expert_count * capacity, -1),
        "tensor", split_axis=0, concat_axis=2, tiled=True,
    )[0]
    expert_sum = jnp.einsum(
        "sh,thc->stc", hidden_own, down_all, preferred_element_type=jnp.float32
    )
    expert_rows = expert_sum.astype(jnp.bfloat16).reshape(expert_count, capacity, feature_width)
    returned = lax.all_to_all(expert_rows, "expert", split_axis=0, concat_axis=0, tiled=True)
    returned = returned.reshape(expert_count, capacity, feature_width)
    pair_weight = jnp.sum(jnp.where(hit, own_weights[..., None], 0.0), axis=1)
    mixing = jnp.where(chosen, pair_weight[..., None], 0.0)
    combined = jnp.einsum(
        "rec,ecd->rd", mixing, returned.astype(jnp.float32), precision=lax.Precision.HIGHEST
    )
    return combined.astype(jnp.bfloat16)


def solution(mesh):
    return jax.shard_map(
        on_device,
        mesh=mesh,
        in_specs=(
            P("tensor", "expert", None),
            P(),
            P("expert", None),
            P("expert", None),
            P("expert", None, "tensor"),
            P("expert", None, "tensor"),
            P("expert", None, "tensor"),
        ),
        out_specs=P(("expert", "tensor"), None),
        check_vma=False,
    )
```

```python
import jax
import jax.numpy as jnp
from jax import lax
from jax.sharding import PartitionSpec as P

QB = 128


def normalize_dequant(summed, norm_gain, block_width):
    row_count, feature_width = summed.shape
    mean_sq = jnp.mean(summed * summed, axis=-1, keepdims=True)
    normed = summed * lax.rsqrt(mean_sq + 1e-06) * norm_gain
    blocks = normed.reshape(row_count, feature_width // block_width, block_width)
    scales = ((jnp.max(jnp.abs(blocks), axis=-1) + 1e-06) / 448.0).astype(jnp.bfloat16)
    scale_f = scales.astype(jnp.float32)[:, :, None]
    values = (blocks / scale_f).astype(jnp.bfloat16)
    restored = (values.astype(jnp.float32) * scale_f).astype(jnp.bfloat16)
    return restored.reshape(row_count, feature_width)


def on_device(attn_partial, norm_gain, expert_ids, route_weights, gate_proj, up_proj, down_proj):
    tensor_count = lax.axis_size("tensor")
    expert_count = lax.axis_size("expert")
    tensor_index = lax.axis_index("tensor")
    group_tokens = expert_ids.shape[0]
    top_count = expert_ids.shape[1]
    row_count = group_tokens // tensor_count
    feature_width = attn_partial.shape[2]
    capacity = max(2, (2 * row_count * top_count + expert_count - 1) // expert_count)
    gate_matrix = gate_proj[0]
    up_matrix = up_proj[0]
    down_matrix = down_proj[0]
    own_start = tensor_index * row_count
    own_ids = lax.dynamic_slice_in_dim(expert_ids, own_start, row_count, 0)
    own_weights = lax.dynamic_slice_in_dim(route_weights, own_start, row_count, 0)

    parts = lax.all_to_all(
        attn_partial[0].reshape(tensor_count, row_count, feature_width),
        "tensor", split_axis=0, concat_axis=0, tiled=True,
    )
    summed = jnp.sum(parts.astype(jnp.float32), axis=0)
    restored = normalize_dequant(summed, norm_gain, QB)

    labels = jnp.arange(expert_count, dtype=jnp.int32)
    hit = own_ids[..., None] == labels
    member = jnp.sum(hit.astype(jnp.int32), axis=1)
    earlier = jnp.cumsum(member, axis=0) - member
    places = jnp.arange(capacity, dtype=jnp.int32)
    chosen = (earlier[..., None] == places) & (member[..., None] > 0)
    send = jnp.einsum(
        "rec,rd->ecd", chosen.astype(jnp.bfloat16), restored, preferred_element_type=jnp.float32
    ).astype(jnp.bfloat16)
    recv = lax.all_to_all(send, "expert", split_axis=0, concat_axis=0, tiled=True)
    forward = [(i, (i + 1) % tensor_count) for i in range(tensor_count)]
    backward = [(i, (i - 1) % tensor_count) for i in range(tensor_count)]
    weight_parts = [down_matrix] + [None] * (tensor_count - 1)
    ahead = down_matrix
    behind = down_matrix
    for step in range(1, tensor_count // 2 + 1):
        ahead = lax.ppermute(ahead, "tensor", forward)
        weight_parts[tensor_count - step] = ahead
        if step < tensor_count - step:
            behind = lax.ppermute(behind, "tensor", backward)
            weight_parts[step] = behind
    down_all = weight_parts
    def front(piece):
        gate_act = jnp.dot(piece, gate_matrix, preferred_element_type=jnp.float32)
        up_act = jnp.dot(piece, up_matrix, preferred_element_type=jnp.float32)
        return (jax.nn.silu(gate_act) * up_act).astype(jnp.bfloat16)

    down_all, recv = lax.optimization_barrier((down_all, recv))
    own_rows = recv.reshape(expert_count * capacity, feature_width)
    hidden_parts = [front(own_rows)] + [None] * (tensor_count - 1)
    ahead = own_rows
    behind = own_rows
    half = own_rows.shape[0] // 2
    for step in range(1, tensor_count // 2 + 1):
        if step < tensor_count - step:
            ahead = lax.ppermute(ahead, "tensor", forward)
            hidden_parts[tensor_count - step] = front(ahead)
            behind = lax.ppermute(behind, "tensor", backward)
            hidden_parts[step] = front(behind)
        else:
            first = lax.ppermute(ahead[:half], "tensor", forward)
            second = lax.ppermute(behind[half:], "tensor", backward)
            hidden_parts[step] = jnp.concatenate([front(first), front(second)], axis=0)
    hidden = jnp.roll(jnp.stack(hidden_parts), tensor_index, axis=0)
    hidden_own = lax.all_to_all(
        hidden.reshape(tensor_count, expert_count * capacity, -1),
        "tensor", split_axis=0, concat_axis=2, tiled=True,
    )[0]
    expert_sum = jnp.einsum(
        "sh,mhc->smc", hidden_own, jnp.stack(down_all), preferred_element_type=jnp.float32
    ).astype(jnp.bfloat16)
    expert_sum = jnp.roll(expert_sum, tensor_index, axis=1)
    expert_rows = expert_sum.reshape(expert_count, capacity, feature_width)
    returned = lax.all_to_all(expert_rows, "expert", split_axis=0, concat_axis=0, tiled=True)
    returned = returned.reshape(expert_count, capacity, feature_width)
    pair_weight = jnp.sum(jnp.where(hit, own_weights[..., None], 0.0), axis=1)
    mixing = jnp.where(chosen, pair_weight[..., None], 0.0)
    combined = jnp.einsum(
        "rec,ecd->rd", mixing, returned.astype(jnp.float32), precision=lax.Precision.HIGHEST
    )
    return combined.astype(jnp.bfloat16)


def solution(mesh):
    return jax.shard_map(
        on_device,
        mesh=mesh,
        in_specs=(
            P("tensor", "expert", None),
            P(),
            P("expert", None),
            P("expert", None),
            P("expert", None, "tensor"),
            P("expert", None, "tensor"),
            P("expert", None, "tensor"),
        ),
        out_specs=P(("expert", "tensor"), None),
        check_vma=False,
    )
```

```python
import jax
import jax.numpy as jnp
from jax import lax
from jax.sharding import PartitionSpec as P

QB = 128


def normalize_dequant(summed, norm_gain, block_width):
    row_count, feature_width = summed.shape
    mean_sq = jnp.mean(summed * summed, axis=-1, keepdims=True)
    normed = summed * lax.rsqrt(mean_sq + 1e-06) * norm_gain
    blocks = normed.reshape(row_count, feature_width // block_width, block_width)
    scales = ((jnp.max(jnp.abs(blocks), axis=-1) + 1e-06) / 448.0).astype(jnp.bfloat16)
    scale_f = scales.astype(jnp.float32)[:, :, None]
    values = (blocks / scale_f).astype(jnp.bfloat16)
    restored = (values.astype(jnp.float32) * scale_f).astype(jnp.bfloat16)
    return restored.reshape(row_count, feature_width)


def on_device(attn_partial, norm_gain, expert_ids, route_weights, gate_proj, up_proj, down_proj):
    tensor_count = lax.axis_size("tensor")
    expert_count = lax.axis_size("expert")
    tensor_index = lax.axis_index("tensor")
    group_tokens = expert_ids.shape[0]
    top_count = expert_ids.shape[1]
    row_count = group_tokens // tensor_count
    feature_width = attn_partial.shape[2]
    capacity = max(2, (2 * row_count * top_count + expert_count - 1) // expert_count)
    gate_matrix = gate_proj[0]
    up_matrix = up_proj[0]
    down_matrix = down_proj[0]
    own_start = tensor_index * row_count
    own_ids = lax.dynamic_slice_in_dim(expert_ids, own_start, row_count, 0)
    own_weights = lax.dynamic_slice_in_dim(route_weights, own_start, row_count, 0)

    parts = lax.all_to_all(
        attn_partial[0].reshape(tensor_count, row_count, feature_width),
        "tensor", split_axis=0, concat_axis=0, tiled=True,
    )
    summed = jnp.sum(parts.astype(jnp.float32), axis=0)
    restored = normalize_dequant(summed, norm_gain, QB)

    labels = jnp.arange(expert_count, dtype=jnp.int32)
    hit = own_ids[..., None] == labels
    member = jnp.sum(hit.astype(jnp.int32), axis=1)
    earlier = jnp.cumsum(member, axis=0) - member
    places = jnp.arange(capacity, dtype=jnp.int32)
    chosen = (earlier[..., None] == places) & (member[..., None] > 0)
    send = jnp.einsum(
        "rec,rd->ecd", chosen.astype(jnp.bfloat16), restored, preferred_element_type=jnp.float32
    ).astype(jnp.bfloat16)
    recv = lax.all_to_all(send, "expert", split_axis=0, concat_axis=0, tiled=True)
    forward = [(i, (i + 1) % tensor_count) for i in range(tensor_count)]
    backward = [(i, (i - 1) % tensor_count) for i in range(tensor_count)]
    weight_parts = [down_matrix] + [None] * (tensor_count - 1)
    ahead = down_matrix
    behind = down_matrix
    for step in range(1, tensor_count // 2 + 1):
        ahead = lax.ppermute(ahead, "tensor", forward)
        weight_parts[tensor_count - step] = ahead
        if step < tensor_count - step:
            behind = lax.ppermute(behind, "tensor", backward)
            weight_parts[step] = behind
    down_all = weight_parts
    def front(piece):
        gate_act = jnp.dot(piece, gate_matrix, preferred_element_type=jnp.float32)
        up_act = jnp.dot(piece, up_matrix, preferred_element_type=jnp.float32)
        return (jax.nn.silu(gate_act) * up_act).astype(jnp.bfloat16)

    down_all, recv = lax.optimization_barrier((down_all, recv))
    own_rows = recv.reshape(expert_count * capacity, feature_width)
    def toward(shift):
        return [(i, (i + shift) % tensor_count) for i in range(tensor_count)]

    received = [front(own_rows)] + [None] * (tensor_count - 1)
    ahead = own_rows
    behind = own_rows
    half = own_rows.shape[0] // 2
    for step in range(1, tensor_count // 2 + 1):
        if step < tensor_count - step:
            ahead = lax.ppermute(ahead, "tensor", forward)
            received[step] = lax.ppermute(front(ahead), "tensor", toward(-step))
            behind = lax.ppermute(behind, "tensor", backward)
            received[tensor_count - step] = lax.ppermute(front(behind), "tensor", toward(step))
        else:
            first = lax.ppermute(ahead[:half], "tensor", forward)
            second = lax.ppermute(behind[half:], "tensor", backward)
            opposite = jnp.concatenate([front(first), front(second)], axis=0)
            received[step] = lax.ppermute(opposite, "tensor", toward(step))
    hidden_own = jnp.roll(jnp.stack(received), tensor_index, axis=0)
    hidden_own = hidden_own.transpose(1, 0, 2).reshape(own_rows.shape[0], -1)
    expert_sum = jnp.einsum(
        "sh,mhc->smc", hidden_own, jnp.stack(down_all), preferred_element_type=jnp.float32
    ).astype(jnp.bfloat16)
    expert_sum = jnp.roll(expert_sum, tensor_index, axis=1)
    expert_rows = expert_sum.reshape(expert_count, capacity, feature_width)
    returned = lax.all_to_all(expert_rows, "expert", split_axis=0, concat_axis=0, tiled=True)
    returned = returned.reshape(expert_count, capacity, feature_width)
    pair_weight = jnp.sum(jnp.where(hit, own_weights[..., None], 0.0), axis=1)
    mixing = jnp.where(chosen, pair_weight[..., None], 0.0)
    combined = jnp.einsum(
        "rec,ecd->rd", mixing, returned.astype(jnp.float32), precision=lax.Precision.HIGHEST
    )
    return combined.astype(jnp.bfloat16)


def solution(mesh):
    return jax.shard_map(
        on_device,
        mesh=mesh,
        in_specs=(
            P("tensor", "expert", None),
            P(),
            P("expert", None),
            P("expert", None),
            P("expert", None, "tensor"),
            P("expert", None, "tensor"),
            P("expert", None, "tensor"),
        ),
        out_specs=P(("expert", "tensor"), None),
        check_vma=False,
    )
```

```python
import jax
import jax.numpy as jnp
from jax import lax
from jax.sharding import PartitionSpec as P

QB = 128


def normalize_dequant(summed, norm_gain, block_width):
    row_count, feature_width = summed.shape
    mean_sq = jnp.mean(summed * summed, axis=-1, keepdims=True)
    normed = summed * lax.rsqrt(mean_sq + 1e-06) * norm_gain
    blocks = normed.reshape(row_count, feature_width // block_width, block_width)
    scales = ((jnp.max(jnp.abs(blocks), axis=-1) + 1e-06) / 448.0).astype(jnp.bfloat16)
    scale_f = scales.astype(jnp.float32)[:, :, None]
    values = (blocks / scale_f).astype(jnp.bfloat16)
    restored = (values.astype(jnp.float32) * scale_f).astype(jnp.bfloat16)
    return restored.reshape(row_count, feature_width)


def on_device(attn_partial, norm_gain, expert_ids, route_weights, gate_proj, up_proj, down_proj):
    tensor_count = lax.axis_size("tensor")
    expert_count = lax.axis_size("expert")
    tensor_index = lax.axis_index("tensor")
    group_tokens = expert_ids.shape[0]
    top_count = expert_ids.shape[1]
    row_count = group_tokens // tensor_count
    feature_width = attn_partial.shape[2]
    capacity = max(2, (2 * row_count * top_count + expert_count - 1) // expert_count)
    gate_matrix = gate_proj[0]
    up_matrix = up_proj[0]
    down_matrix = down_proj[0]
    own_start = tensor_index * row_count
    own_ids = lax.dynamic_slice_in_dim(expert_ids, own_start, row_count, 0)
    own_weights = lax.dynamic_slice_in_dim(route_weights, own_start, row_count, 0)

    parts = lax.all_to_all(
        attn_partial[0].reshape(tensor_count, row_count, feature_width),
        "tensor", split_axis=0, concat_axis=0, tiled=True,
    )
    summed = jnp.sum(parts.astype(jnp.float32), axis=0)
    restored = normalize_dequant(summed, norm_gain, QB)

    labels = jnp.arange(expert_count, dtype=jnp.int32)
    hit = own_ids[..., None] == labels
    member = jnp.sum(hit.astype(jnp.int32), axis=1)
    earlier = jnp.cumsum(member, axis=0) - member
    places = jnp.arange(capacity, dtype=jnp.int32)
    chosen = (earlier[..., None] == places) & (member[..., None] > 0)
    send = jnp.einsum(
        "rec,rd->ecd", chosen.astype(jnp.bfloat16), restored, preferred_element_type=jnp.float32
    ).astype(jnp.bfloat16)
    recv = lax.all_to_all(send, "expert", split_axis=0, concat_axis=0, tiled=True)
    forward = [(i, (i + 1) % tensor_count) for i in range(tensor_count)]
    backward = [(i, (i - 1) % tensor_count) for i in range(tensor_count)]
    weight_parts = [down_matrix] + [None] * (tensor_count - 1)
    ahead = down_matrix
    behind = down_matrix
    share = down_matrix.shape[0] // 2
    for step in range(1, tensor_count // 2 + 1):
        if step < tensor_count - step:
            ahead = lax.ppermute(ahead, "tensor", forward)
            weight_parts[tensor_count - step] = ahead
            behind = lax.ppermute(behind, "tensor", backward)
            weight_parts[step] = behind
        else:
            weight_parts[step] = jnp.concatenate(
                [
                    lax.ppermute(ahead[:share], "tensor", forward),
                    lax.ppermute(behind[share:], "tensor", backward),
                ],
                axis=0,
            )
    down_all = weight_parts
    def front(piece):
        gate_act = jnp.dot(piece, gate_matrix, preferred_element_type=jnp.float32)
        up_act = jnp.dot(piece, up_matrix, preferred_element_type=jnp.float32)
        return (jax.nn.silu(gate_act) * up_act).astype(jnp.bfloat16)

    down_all, recv = lax.optimization_barrier((down_all, recv))
    own_rows = recv.reshape(expert_count * capacity, feature_width)
    hidden_parts = [front(own_rows)] + [None] * (tensor_count - 1)
    ahead = own_rows
    behind = own_rows
    half = own_rows.shape[0] // 2
    for step in range(1, tensor_count // 2 + 1):
        if step < tensor_count - step:
            ahead = lax.ppermute(ahead, "tensor", forward)
            hidden_parts[tensor_count - step] = front(ahead)
            behind = lax.ppermute(behind, "tensor", backward)
            hidden_parts[step] = front(behind)
        else:
            first = lax.ppermute(ahead[:half], "tensor", forward)
            second = lax.ppermute(behind[half:], "tensor", backward)
            hidden_parts[step] = jnp.concatenate([front(first), front(second)], axis=0)
    hidden = jnp.roll(jnp.stack(hidden_parts), tensor_index, axis=0)
    hidden_own = lax.all_to_all(
        hidden.reshape(tensor_count, expert_count * capacity, -1),
        "tensor", split_axis=0, concat_axis=2, tiled=True,
    )[0]
    expert_sum = jnp.einsum(
        "sh,mhc->smc", hidden_own, jnp.stack(down_all), preferred_element_type=jnp.float32
    ).astype(jnp.bfloat16)
    expert_sum = jnp.roll(expert_sum, tensor_index, axis=1)
    expert_rows = expert_sum.reshape(expert_count, capacity, feature_width)
    returned = lax.all_to_all(expert_rows, "expert", split_axis=0, concat_axis=0, tiled=True)
    returned = returned.reshape(expert_count, capacity, feature_width)
    pair_weight = jnp.sum(jnp.where(hit, own_weights[..., None], 0.0), axis=1)
    mixing = jnp.where(chosen, pair_weight[..., None], 0.0)
    combined = jnp.einsum(
        "rec,ecd->rd", mixing, returned.astype(jnp.float32), precision=lax.Precision.HIGHEST
    )
    return combined.astype(jnp.bfloat16)


def solution(mesh):
    return jax.shard_map(
        on_device,
        mesh=mesh,
        in_specs=(
            P("tensor", "expert", None),
            P(),
            P("expert", None),
            P("expert", None),
            P("expert", None, "tensor"),
            P("expert", None, "tensor"),
            P("expert", None, "tensor"),
        ),
        out_specs=P(("expert", "tensor"), None),
        check_vma=False,
    )
```

```python
import jax
import jax.numpy as jnp
from jax import lax
from jax.sharding import PartitionSpec as P

QB = 128


def normalize_dequant(summed, norm_gain, block_width):
    row_count, feature_width = summed.shape
    mean_sq = jnp.mean(summed * summed, axis=-1, keepdims=True)
    normed = summed * lax.rsqrt(mean_sq + 1e-06) * norm_gain
    blocks = normed.reshape(row_count, feature_width // block_width, block_width)
    scales = ((jnp.max(jnp.abs(blocks), axis=-1) + 1e-06) / 448.0).astype(jnp.bfloat16)
    scale_f = scales.astype(jnp.float32)[:, :, None]
    values = (blocks / scale_f).astype(jnp.bfloat16)
    restored = (values.astype(jnp.float32) * scale_f).astype(jnp.bfloat16)
    return restored.reshape(row_count, feature_width)


def on_device(attn_partial, norm_gain, expert_ids, route_weights, gate_proj, up_proj, down_proj):
    tensor_count = lax.axis_size("tensor")
    expert_count = lax.axis_size("expert")
    tensor_index = lax.axis_index("tensor")
    group_tokens = expert_ids.shape[0]
    top_count = expert_ids.shape[1]
    row_count = group_tokens // tensor_count
    feature_width = attn_partial.shape[2]
    capacity = max(2, (2 * row_count * top_count + expert_count - 1) // expert_count)
    gate_matrix = gate_proj[0]
    up_matrix = up_proj[0]
    down_matrix = down_proj[0]
    own_start = tensor_index * row_count
    own_ids = lax.dynamic_slice_in_dim(expert_ids, own_start, row_count, 0)
    own_weights = lax.dynamic_slice_in_dim(route_weights, own_start, row_count, 0)

    parts = lax.all_to_all(
        attn_partial[0].reshape(tensor_count, row_count, feature_width),
        "tensor", split_axis=0, concat_axis=0, tiled=True,
    )
    summed = jnp.sum(parts.astype(jnp.float32), axis=0)
    restored = normalize_dequant(summed, norm_gain, QB)

    labels = jnp.arange(expert_count, dtype=jnp.int32)
    hit = own_ids[..., None] == labels
    member = jnp.sum(hit.astype(jnp.int32), axis=1)
    earlier = jnp.cumsum(member, axis=0) - member
    places = jnp.arange(capacity, dtype=jnp.int32)
    chosen = (earlier[..., None] == places) & (member[..., None] > 0)
    send = jnp.einsum(
        "rec,rd->ecd", chosen.astype(jnp.bfloat16), restored, preferred_element_type=jnp.float32
    ).astype(jnp.bfloat16)
    recv = lax.all_to_all(send, "expert", split_axis=0, concat_axis=0, tiled=True)
    forward = [(i, (i + 1) % tensor_count) for i in range(tensor_count)]
    backward = [(i, (i - 1) % tensor_count) for i in range(tensor_count)]
    weight_parts = [down_matrix] + [None] * (tensor_count - 1)
    ahead = down_matrix
    behind = down_matrix
    for step in range(1, tensor_count // 2 + 1):
        ahead = lax.ppermute(ahead, "tensor", forward)
        weight_parts[tensor_count - step] = ahead
        if step < tensor_count - step:
            behind = lax.ppermute(behind, "tensor", backward)
            weight_parts[step] = behind
    down_all = weight_parts
    def front(piece):
        gate_act = jnp.dot(piece, gate_matrix, preferred_element_type=jnp.float32)
        up_act = jnp.dot(piece, up_matrix, preferred_element_type=jnp.float32)
        return (jax.nn.silu(gate_act) * up_act).astype(jnp.bfloat16)

    own_rows = recv.reshape(expert_count * capacity, feature_width)
    hidden_parts = [front(own_rows)] + [None] * (tensor_count - 1)
    ahead = own_rows
    behind = own_rows
    half = own_rows.shape[0] // 2
    for step in range(1, tensor_count // 2 + 1):
        if step < tensor_count - step:
            ahead = lax.ppermute(ahead, "tensor", forward)
            hidden_parts[tensor_count - step] = front(ahead)
            behind = lax.ppermute(behind, "tensor", backward)
            hidden_parts[step] = front(behind)
        else:
            first = lax.ppermute(ahead[:half], "tensor", forward)
            second = lax.ppermute(behind[half:], "tensor", backward)
            hidden_parts[step] = jnp.concatenate([front(first), front(second)], axis=0)
    hidden = jnp.roll(jnp.stack(hidden_parts), tensor_index, axis=0)
    hidden_own = lax.all_to_all(
        hidden.reshape(tensor_count, expert_count * capacity, -1),
        "tensor", split_axis=0, concat_axis=2, tiled=True,
    )[0]
    expert_sum = jnp.einsum(
        "sh,mhc->smc", hidden_own, jnp.stack(down_all), preferred_element_type=jnp.float32
    ).astype(jnp.bfloat16)
    expert_sum = jnp.roll(expert_sum, tensor_index, axis=1)
    expert_rows = expert_sum.reshape(expert_count, capacity, feature_width)
    returned = lax.all_to_all(expert_rows, "expert", split_axis=0, concat_axis=0, tiled=True)
    returned = returned.reshape(expert_count, capacity, feature_width)
    pair_weight = jnp.sum(jnp.where(hit, own_weights[..., None], 0.0), axis=1)
    mixing = jnp.where(chosen, pair_weight[..., None], 0.0)
    combined = jnp.einsum(
        "rec,ecd->rd", mixing, returned.astype(jnp.float32), precision=lax.Precision.HIGHEST
    )
    return combined.astype(jnp.bfloat16)


def solution(mesh):
    return jax.shard_map(
        on_device,
        mesh=mesh,
        in_specs=(
            P("tensor", "expert", None),
            P(),
            P("expert", None),
            P("expert", None),
            P("expert", None, "tensor"),
            P("expert", None, "tensor"),
            P("expert", None, "tensor"),
        ),
        out_specs=P(("expert", "tensor"), None),
        check_vma=False,
    )
```

```python
import jax
import jax.numpy as jnp
from jax import lax
from jax.sharding import PartitionSpec as P

QB = 128


def normalize_dequant(summed, norm_gain, block_width):
    row_count, feature_width = summed.shape
    mean_sq = jnp.mean(summed * summed, axis=-1, keepdims=True)
    normed = summed * lax.rsqrt(mean_sq + 1e-06) * norm_gain
    blocks = normed.reshape(row_count, feature_width // block_width, block_width)
    scales = ((jnp.max(jnp.abs(blocks), axis=-1) + 1e-06) / 448.0).astype(jnp.bfloat16)
    scale_f = scales.astype(jnp.float32)[:, :, None]
    values = (blocks / scale_f).astype(jnp.bfloat16)
    restored = (values.astype(jnp.float32) * scale_f).astype(jnp.bfloat16)
    return restored.reshape(row_count, feature_width)


def on_device(attn_partial, norm_gain, expert_ids, route_weights, gate_proj, up_proj, down_proj):
    tensor_count = lax.axis_size("tensor")
    expert_count = lax.axis_size("expert")
    tensor_index = lax.axis_index("tensor")
    group_tokens = expert_ids.shape[0]
    top_count = expert_ids.shape[1]
    row_count = group_tokens // tensor_count
    feature_width = attn_partial.shape[2]
    capacity = max(2, (2 * row_count * top_count + expert_count - 1) // expert_count)
    gate_matrix = gate_proj[0]
    up_matrix = up_proj[0]
    down_matrix = down_proj[0]
    own_start = tensor_index * row_count
    own_ids = lax.dynamic_slice_in_dim(expert_ids, own_start, row_count, 0)
    own_weights = lax.dynamic_slice_in_dim(route_weights, own_start, row_count, 0)

    parts = lax.all_to_all(
        attn_partial[0].reshape(tensor_count, row_count, feature_width),
        "tensor", split_axis=0, concat_axis=0, tiled=True,
    )
    summed = jnp.sum(parts.astype(jnp.float32), axis=0)
    restored = normalize_dequant(summed, norm_gain, QB)

    labels = jnp.arange(expert_count, dtype=jnp.int32)
    hit = own_ids[..., None] == labels
    member = jnp.sum(hit.astype(jnp.int32), axis=1)
    earlier = jnp.cumsum(member, axis=0) - member
    places = jnp.arange(capacity, dtype=jnp.int32)
    chosen = (earlier[..., None] == places) & (member[..., None] > 0)
    send = jnp.einsum(
        "rec,rd->ecd", chosen.astype(jnp.bfloat16), restored, preferred_element_type=jnp.float32
    ).astype(jnp.bfloat16)
    recv = lax.all_to_all(send, "expert", split_axis=0, concat_axis=0, tiled=True)
    forward = [(i, (i + 1) % tensor_count) for i in range(tensor_count)]
    backward = [(i, (i - 1) % tensor_count) for i in range(tensor_count)]
    weight_parts = [down_matrix] + [None] * (tensor_count - 1)
    ahead = down_matrix
    behind = down_matrix
    for step in range(1, tensor_count // 2 + 1):
        ahead = lax.ppermute(ahead, "tensor", forward)
        weight_parts[tensor_count - step] = ahead
        if step < tensor_count - step:
            behind = lax.ppermute(behind, "tensor", backward)
            weight_parts[step] = behind
    down_all = weight_parts
    def front(piece):
        gate_act = jnp.dot(piece, gate_matrix, preferred_element_type=jnp.float32)
        up_act = jnp.dot(piece, up_matrix, preferred_element_type=jnp.float32)
        return (jax.nn.silu(gate_act) * up_act).astype(jnp.bfloat16)

    down_all, recv = lax.optimization_barrier((down_all, recv))
    down_abs = jnp.roll(jnp.stack(down_all), tensor_index, axis=0)
    own_rows = recv.reshape(expert_count * capacity, feature_width)
    hidden_parts = [front(own_rows)] + [None] * (tensor_count - 1)
    ahead = own_rows
    behind = own_rows
    half = own_rows.shape[0] // 2
    for step in range(1, tensor_count // 2 + 1):
        if step < tensor_count - step:
            ahead = lax.ppermute(ahead, "tensor", forward)
            hidden_parts[tensor_count - step] = front(ahead)
            behind = lax.ppermute(behind, "tensor", backward)
            hidden_parts[step] = front(behind)
        else:
            first = lax.ppermute(ahead[:half], "tensor", forward)
            second = lax.ppermute(behind[half:], "tensor", backward)
            hidden_parts[step] = jnp.concatenate([front(first), front(second)], axis=0)
    hidden = jnp.roll(jnp.stack(hidden_parts), tensor_index, axis=0)
    hidden_own = lax.all_to_all(
        hidden.reshape(tensor_count, expert_count * capacity, -1),
        "tensor", split_axis=0, concat_axis=2, tiled=True,
    )[0]
    expert_sum = jnp.einsum(
        "sh,jhc->sjc", hidden_own, down_abs, preferred_element_type=jnp.float32
    ).astype(jnp.bfloat16)
    expert_rows = expert_sum.reshape(expert_count, capacity, feature_width)
    returned = lax.all_to_all(expert_rows, "expert", split_axis=0, concat_axis=0, tiled=True)
    returned = returned.reshape(expert_count, capacity, feature_width)
    pair_weight = jnp.sum(jnp.where(hit, own_weights[..., None], 0.0), axis=1)
    mixing = jnp.where(chosen, pair_weight[..., None], 0.0)
    combined = jnp.einsum(
        "rec,ecd->rd", mixing, returned.astype(jnp.float32), precision=lax.Precision.HIGHEST
    )
    return combined.astype(jnp.bfloat16)


def solution(mesh):
    return jax.shard_map(
        on_device,
        mesh=mesh,
        in_specs=(
            P("tensor", "expert", None),
            P(),
            P("expert", None),
            P("expert", None),
            P("expert", None, "tensor"),
            P("expert", None, "tensor"),
            P("expert", None, "tensor"),
        ),
        out_specs=P(("expert", "tensor"), None),
        check_vma=False,
    )
```

```python
import jax
import jax.numpy as jnp
from jax import lax
from jax.sharding import PartitionSpec as P

QB = 128


def normalize_dequant(summed, norm_gain, block_width):
    row_count, feature_width = summed.shape
    mean_sq = jnp.mean(summed * summed, axis=-1, keepdims=True)
    normed = summed * lax.rsqrt(mean_sq + 1e-06) * norm_gain
    blocks = normed.reshape(row_count, feature_width // block_width, block_width)
    scales = ((jnp.max(jnp.abs(blocks), axis=-1) + 1e-06) / 448.0).astype(jnp.bfloat16)
    scale_f = scales.astype(jnp.float32)[:, :, None]
    values = (blocks / scale_f).astype(jnp.bfloat16)
    restored = (values.astype(jnp.float32) * scale_f).astype(jnp.bfloat16)
    return restored.reshape(row_count, feature_width)


def on_device(attn_partial, norm_gain, expert_ids, route_weights, gate_proj, up_proj, down_proj):
    tensor_count = lax.axis_size("tensor")
    expert_count = lax.axis_size("expert")
    tensor_index = lax.axis_index("tensor")
    group_tokens = expert_ids.shape[0]
    top_count = expert_ids.shape[1]
    row_count = group_tokens // tensor_count
    feature_width = attn_partial.shape[2]
    capacity = max(2, (2 * row_count * top_count + expert_count - 1) // expert_count)
    gate_matrix = gate_proj[0]
    up_matrix = up_proj[0]
    down_matrix = down_proj[0]
    own_start = tensor_index * row_count
    own_ids = lax.dynamic_slice_in_dim(expert_ids, own_start, row_count, 0)
    own_weights = lax.dynamic_slice_in_dim(route_weights, own_start, row_count, 0)

    parts = lax.all_to_all(
        attn_partial[0].reshape(tensor_count, row_count, feature_width),
        "tensor", split_axis=0, concat_axis=0, tiled=True,
    )
    down_first, parts = lax.optimization_barrier((down_matrix, parts))
    summed = jnp.sum(parts.astype(jnp.float32), axis=0)
    restored = normalize_dequant(summed, norm_gain, QB)

    labels = jnp.arange(expert_count, dtype=jnp.int32)
    hit = own_ids[..., None] == labels
    member = jnp.sum(hit.astype(jnp.int32), axis=1)
    earlier = jnp.cumsum(member, axis=0) - member
    places = jnp.arange(capacity, dtype=jnp.int32)
    chosen = (earlier[..., None] == places) & (member[..., None] > 0)
    send = jnp.einsum(
        "rec,rd->ecd", chosen.astype(jnp.bfloat16), restored, preferred_element_type=jnp.float32
    ).astype(jnp.bfloat16)
    recv = lax.all_to_all(send, "expert", split_axis=0, concat_axis=0, tiled=True)
    forward = [(i, (i + 1) % tensor_count) for i in range(tensor_count)]
    backward = [(i, (i - 1) % tensor_count) for i in range(tensor_count)]
    weight_parts = [down_first] + [None] * (tensor_count - 1)
    ahead = down_first
    behind = down_first
    for step in range(1, tensor_count // 2 + 1):
        ahead = lax.ppermute(ahead, "tensor", forward)
        weight_parts[tensor_count - step] = ahead
        if step < tensor_count - step:
            behind = lax.ppermute(behind, "tensor", backward)
            weight_parts[step] = behind
    down_all = weight_parts
    def front(piece):
        gate_act = jnp.dot(piece, gate_matrix, preferred_element_type=jnp.float32)
        up_act = jnp.dot(piece, up_matrix, preferred_element_type=jnp.float32)
        return (jax.nn.silu(gate_act) * up_act).astype(jnp.bfloat16)

    down_all, recv = lax.optimization_barrier((down_all, recv))
    own_rows = recv.reshape(expert_count * capacity, feature_width)
    hidden_parts = [front(own_rows)] + [None] * (tensor_count - 1)
    ahead = own_rows
    behind = own_rows
    half = own_rows.shape[0] // 2
    for step in range(1, tensor_count // 2 + 1):
        if step < tensor_count - step:
            ahead = lax.ppermute(ahead, "tensor", forward)
            hidden_parts[tensor_count - step] = front(ahead)
            behind = lax.ppermute(behind, "tensor", backward)
            hidden_parts[step] = front(behind)
        else:
            first = lax.ppermute(ahead[:half], "tensor", forward)
            second = lax.ppermute(behind[half:], "tensor", backward)
            hidden_parts[step] = jnp.concatenate([front(first), front(second)], axis=0)
    hidden = jnp.roll(jnp.stack(hidden_parts), tensor_index, axis=0)
    hidden_own = lax.all_to_all(
        hidden.reshape(tensor_count, expert_count * capacity, -1),
        "tensor", split_axis=0, concat_axis=2, tiled=True,
    )[0]
    expert_sum = jnp.einsum(
        "sh,mhc->smc", hidden_own, jnp.stack(down_all), preferred_element_type=jnp.float32
    ).astype(jnp.bfloat16)
    expert_sum = jnp.roll(expert_sum, tensor_index, axis=1)
    expert_rows = expert_sum.reshape(expert_count, capacity, feature_width)
    returned = lax.all_to_all(expert_rows, "expert", split_axis=0, concat_axis=0, tiled=True)
    returned = returned.reshape(expert_count, capacity, feature_width)
    pair_weight = jnp.sum(jnp.where(hit, own_weights[..., None], 0.0), axis=1)
    mixing = jnp.where(chosen, pair_weight[..., None], 0.0)
    combined = jnp.einsum(
        "rec,ecd->rd", mixing, returned.astype(jnp.float32), precision=lax.Precision.HIGHEST
    )
    return combined.astype(jnp.bfloat16)


def solution(mesh):
    return jax.shard_map(
        on_device,
        mesh=mesh,
        in_specs=(
            P("tensor", "expert", None),
            P(),
            P("expert", None),
            P("expert", None),
            P("expert", None, "tensor"),
            P("expert", None, "tensor"),
            P("expert", None, "tensor"),
        ),
        out_specs=P(("expert", "tensor"), None),
        check_vma=False,
    )
```
